256 devices in a mesh: blk: 16 (over z, x_lo), dp: 16 (over x_hi, y, core).
Axes of the slice: x: 4 (x_hi: 2, x_lo: 2; x = x_hi * 2 + x_lo), y: 4, z: 8, core: 2. Of those that a mesh axis runs over, the one named last changes fastest.
Arguments:
- audio_frames: bfloat16 [16, 1024, 16, 1024], P('dp', 'blk'), may hold values from -6 to 6
- conv_weight: bfloat16 [3072, 1024], replicated, may hold values from -0.109375 to 0.109375
- proj_weight: bfloat16 [1024, 512], replicated, may hold values from -0.1875 to 0.1875
- text_embed: bfloat16 [16, 1024, 512], P('dp', 'blk'), may hold values from -6 to 6
- pair_langs: int32 [16, 1024], P('dp', 'blk'), may hold values from 0 to 99, as said below
- log_scale: float32 [100], replicated, may hold values from 2 to 5
- lang_bias: float32 [100], replicated, may hold values from 95 to 105
- log_var: float32 [100], replicated, may hold values from -1 to 1
Outputs:
- loss: float32 [], replicated
- scale_grad: float32 [100], replicated
- var_grad: float32 [100], replicated
- conv_grad: float32 [3072, 1024], P('blk', 'dp')
- proj_grad: float32 [1024, 512], P('blk', 'dp')
- text_grad: float32 [16, 1024, 512], P('dp', 'blk')
The draws below stay inside these ranges and needn't reach their ends.
Inputs may be any that keep to these rules, and one draw needn't show every extreme that they name: `pair_langs`: language ids of the pairs; in every draw some languages are named by no pair.
All inputs are finite; a program needn't handle non-finite values.
Results may differ from the reference program's by a relative error of at most 0.029.
Values may be sent and summed in bfloat16 or wider, within the bound.
No kernel may reach another device: no remote copies, remote signals or barrier semaphores. Data moves between devices by JAX's collectives and lax.ppermute only.
A program may use at most 128 MiB of HBM per device.

```python
import jax
import jax.numpy as jnp
from jax import lax

CIN = 1024
WIDTH = 1024
EMB = 512
LANGS = 100
FRAMES = 16
GROUP = 1024
N_DP = 16


def draw_pair_langs(key, part):
    order_key, first_key, second_key = jax.random.split(jax.random.fold_in(key, 17), 3)
    language_order = jax.random.permutation(order_key, LANGS).astype(jnp.int32)
    first_pick = jax.random.randint(first_key, (N_DP, GROUP), 0, LANGS - 3, dtype=jnp.int32)
    second_pick = jax.random.randint(second_key, (N_DP, GROUP), 0, LANGS - 3, dtype=jnp.int32)
    rank_index = jnp.minimum(first_pick, second_pick) + 3
    return jnp.take(language_order, rank_index).astype(jnp.int32)


def level_of(stream_key, extent, cuts, least, high):
    def one(axis_at, parts):
        heights = jax.random.uniform(jax.random.fold_in(jax.random.fold_in(stream_key, 6), axis_at), (parts,), jnp.float32, least / len(cuts), high / len(cuts))
        return jnp.repeat(jnp.exp(heights), extent[axis_at] // parts).reshape((-1,) + (1,) * (len(extent) - axis_at - 1))

    factor_of = one(*cuts[0])
    for cut in cuts[1:]:
        factor_of = factor_of * one(*cut)
    return factor_of


def centred(key, extent, scale, reach, pieces=(), held_as=jnp.bfloat16):
    drawn = jax.random.normal(key, extent, jnp.float32) * scale
    if len(pieces) > 0:
        drawn = level_of(key, extent, pieces, -0.22, 0.18) * drawn
    return jnp.clip(drawn, min=-reach, max=reach).astype(held_as)


def setup_inputs(seed: int = 0) -> dict:
    key_list = jax.random.split(jax.random.key(seed), 9)
    audio_frames = centred(key_list[0], (N_DP, GROUP, FRAMES, CIN), 1.0, 6.0, ((0, 16), (1, 16)))
    conv_weight = centred(key_list[1], (3 * CIN, WIDTH), (3 * CIN) ** -0.5, 0.109375)
    proj_weight = centred(key_list[2], (WIDTH, EMB), WIDTH ** -0.5, 0.1875)
    text_embed = centred(key_list[3], (N_DP, GROUP, EMB), 1.0, 6.0, ((0, 16), (1, 16)))
    pair_langs = draw_pair_langs(jax.random.fold_in(key_list[8], 71), 0)
    log_scale = jnp.clip(jax.random.uniform(key_list[5], (LANGS,), jnp.float32, 2.0, 5.0), 2.0, 5.0)
    lang_bias = jnp.clip(jax.random.uniform(key_list[6], (LANGS,), jnp.float32, 95.0, 105.0), 95.0, 105.0)
    log_var = jnp.clip(jax.random.uniform(key_list[7], (LANGS,), jnp.float32, -1.0, 1.0), -1.0, 1.0)
    return dict(audio_frames=audio_frames, conv_weight=conv_weight, proj_weight=proj_weight, text_embed=text_embed, pair_langs=pair_langs, log_scale=log_scale, lang_bias=lang_bias, log_var=log_var)


epsilon = 1e-06

def stack_taps(frames):
    clips, steps_count, channels = frames.shape
    blank = jnp.zeros_like(frames[:, :1])
    before = jnp.concatenate([blank, frames[:, :-1]], axis=1)
    after = jnp.concatenate([frames[:, 1:], blank], axis=1)
    return jnp.concatenate([before, frames, after], axis=2).reshape(clips * steps_count, 3 * channels)

def encode(frames, conv_weight, proj_weight):
    clips, steps_count, channels = frames.shape
    stacked = stack_taps(frames)
    preact = jnp.dot(stacked, conv_weight, preferred_element_type=jnp.float32)
    pooled = lax.optimization_barrier(jnp.mean(jax.nn.gelu(preact).reshape(clips, steps_count, -1), axis=1)).astype(jnp.bfloat16)
    embedding = jnp.dot(pooled, proj_weight, preferred_element_type=jnp.float32)
    audio_len = jnp.sqrt(lax.optimization_barrier(jnp.sum(embedding * embedding, axis=-1, keepdims=True)) + epsilon)
    return (stacked, preact, pooled, embedding / audio_len, audio_len)

def normalize_text(text_rows):
    text_float = text_rows.astype(jnp.float32)
    text_len = jnp.sqrt(lax.optimization_barrier(jnp.sum(text_float * text_float, axis=-1, keepdims=True)) + epsilon)
    return (text_float / text_len, text_len)

def encode_back(stacked, preact, pooled, audio_unit, audio_len, grad_audio, proj_weight):
    clips = pooled.shape[0]
    steps_count = preact.shape[0] // clips
    radial = lax.optimization_barrier(jnp.sum(audio_unit * grad_audio, axis=-1, keepdims=True))
    grad_embed = ((grad_audio - audio_unit * radial) / audio_len).astype(jnp.bfloat16)
    proj_term = lax.dot_general(pooled, grad_embed, (((0,), (0,)), ((), ())), preferred_element_type=jnp.float32)
    grad_pooled = lax.dot_general(grad_embed, proj_weight, (((1,), (1,)), ((), ())), preferred_element_type=jnp.float32) / steps_count
    grad_act = jnp.broadcast_to(grad_pooled[:, None, :], (clips, steps_count, grad_pooled.shape[1])).reshape(clips * steps_count, -1)
    grad_pre = jax.vjp(jax.nn.gelu, preact)[1](grad_act)[0].astype(jnp.bfloat16)
    conv_term = lax.dot_general(stacked, grad_pre, (((0,), (0,)), ((), ())), preferred_element_type=jnp.float32)
    return (conv_term, proj_term)

def reference(audio_frames, conv_weight, proj_weight, text_embed, pair_langs, log_scale, lang_bias, log_var):
    classes = jnp.arange(LANGS, dtype=jnp.int32)
    onehot_all = (pair_langs.reshape(-1)[:, None] == classes[None, :]).astype(jnp.float32)
    counts = lax.optimization_barrier(jnp.sum(onehot_all, axis=0))
    weight_table = jnp.exp(-log_var) / jnp.maximum(counts, 1.0)
    scale_table = jnp.exp(log_scale)

    def one_group(carry, group_data):
        conv_sum, proj_sum, loss_sum, scale_sum = carry
        frames, text_rows, pair_ids = group_data
        stacked, preact, pooled, audio_unit, audio_len = encode(frames, conv_weight, proj_weight)
        audio_bf = audio_unit.astype(jnp.bfloat16)
        text_unit, text_len = normalize_text(text_rows)
        text_bf = text_unit.astype(jnp.bfloat16)
        onehot = (pair_ids[:, None] == classes[None, :]).astype(jnp.float32)
        pair_scale = lax.optimization_barrier(jnp.sum(onehot * scale_table[None, :], axis=1))
        pair_bias = lax.optimization_barrier(jnp.sum(onehot * lang_bias[None, :], axis=1))
        own_weight = lax.optimization_barrier(jnp.sum(onehot * weight_table[None, :], axis=1))
        logits = pair_scale[:, None] * lax.dot_general(audio_bf, text_bf, (((1,), (1,)), ((), ())), preferred_element_type=jnp.float32) + pair_bias[:, None]
        row_max = lax.optimization_barrier(jnp.max(logits, axis=1))
        row_lse = row_max + jnp.log(lax.optimization_barrier(jnp.sum(jnp.exp(logits - row_max[:, None]), axis=1)))
        col_max = lax.optimization_barrier(jnp.max(logits, axis=0))
        col_lse = col_max + jnp.log(lax.optimization_barrier(jnp.sum(jnp.exp(logits - col_max[None, :]), axis=0)))
        positive = jnp.diagonal(logits)
        pair_loss = 0.5 * (row_lse + col_lse) - positive
        rows_index = jnp.arange(logits.shape[0], dtype=jnp.int32)
        on_diagonal = rows_index[:, None] == rows_index[None, :]
        score_grad = 0.5 * (own_weight[:, None] * jnp.exp(logits - row_lse[:, None]) + own_weight[None, :] * jnp.exp(logits - col_lse[None, :]))
        score_grad = score_grad - jnp.where(on_diagonal, own_weight[:, None], 0.0)
        scale_terms = lax.optimization_barrier(jnp.sum(score_grad * (logits - pair_bias[:, None]), axis=1))
        weighted = (score_grad * pair_scale[:, None]).astype(jnp.bfloat16)
        grad_audio = jnp.dot(weighted, text_bf, preferred_element_type=jnp.float32)
        grad_text = lax.dot_general(weighted, audio_bf, (((0,), (0,)), ((), ())), preferred_element_type=jnp.float32)
        text_grad = (grad_text - text_unit * lax.optimization_barrier(jnp.sum(text_unit * grad_text, axis=1, keepdims=True))) / text_len
        conv_term, proj_term = encode_back(stacked, preact, pooled, audio_unit, audio_len, grad_audio, proj_weight)
        loss_sum = loss_sum + lax.optimization_barrier(jnp.sum(onehot * pair_loss[:, None], axis=0))
        scale_sum = scale_sum + lax.optimization_barrier(jnp.sum(onehot * scale_terms[:, None], axis=0))
        return ((conv_sum + conv_term, proj_sum + proj_term, loss_sum, scale_sum), text_grad)
    start_carry = (jnp.zeros((3 * CIN, WIDTH), jnp.float32), jnp.zeros((WIDTH, EMB), jnp.float32), jnp.zeros((LANGS,), jnp.float32), jnp.zeros((LANGS,), jnp.float32))
    final_carry, text_grad = lax.scan(one_group, start_carry, (audio_frames, text_embed, pair_langs))
    conv_grad, proj_grad, loss_sum, scale_grad = final_carry
    var_weight = jnp.exp(-log_var)
    lang_mean = loss_sum / jnp.maximum(counts, 1.0)
    loss = jnp.sum(var_weight * lang_mean + log_var)
    var_grad = 1.0 - var_weight * lang_mean
    return (loss, scale_grad, var_grad, conv_grad, proj_grad, text_grad)
```

```python
import jax
import jax.numpy as jnp
from jax import lax
from jax.sharding import PartitionSpec as P

epsilon = 1e-06


def stack_taps(frames):
    clips, steps_count, channels = frames.shape
    blank = jnp.zeros_like(frames[:, :1])
    before = jnp.concatenate([blank, frames[:, :-1]], axis=1)
    after = jnp.concatenate([frames[:, 1:], blank], axis=1)
    return jnp.concatenate([before, frames, after], axis=2).reshape(
        clips * steps_count, 3 * channels
    )


def encode(frames, conv_weight, proj_weight):
    clips, steps_count, channels = frames.shape
    stacked = stack_taps(frames)
    preact = jnp.dot(stacked, conv_weight, preferred_element_type=jnp.float32)
    pooled = jnp.mean(jax.nn.gelu(preact).reshape(clips, steps_count, -1), axis=1).astype(
        jnp.bfloat16
    )
    embedding = jnp.dot(pooled, proj_weight, preferred_element_type=jnp.float32)
    audio_len = jnp.sqrt(jnp.sum(embedding * embedding, axis=-1, keepdims=True) + epsilon)
    return (stacked, preact, pooled, embedding / audio_len, audio_len)


def normalize_text(text_rows):
    text_float = text_rows.astype(jnp.float32)
    text_len = jnp.sqrt(jnp.sum(text_float * text_float, axis=-1, keepdims=True) + epsilon)
    return (text_float / text_len, text_len)


def encode_back(stacked, preact, pooled, audio_unit, audio_len, grad_audio, proj_weight):
    clips = pooled.shape[0]
    steps_count = preact.shape[0] // clips
    radial = jnp.sum(audio_unit * grad_audio, axis=-1, keepdims=True)
    grad_embed = ((grad_audio - audio_unit * radial) / audio_len).astype(jnp.bfloat16)
    proj_term = lax.dot_general(
        pooled, grad_embed, (((0,), (0,)), ((), ())), preferred_element_type=jnp.float32
    )
    grad_pooled = (
        lax.dot_general(
            grad_embed, proj_weight, (((1,), (1,)), ((), ())), preferred_element_type=jnp.float32
        )
        / steps_count
    )
    grad_act = jnp.broadcast_to(
        grad_pooled[:, None, :], (clips, steps_count, grad_pooled.shape[1])
    ).reshape(clips * steps_count, -1)
    grad_pre = jax.vjp(jax.nn.gelu, preact)[1](grad_act)[0].astype(jnp.bfloat16)
    conv_term = lax.dot_general(
        stacked, grad_pre, (((0,), (0,)), ((), ())), preferred_element_type=jnp.float32
    )
    return (conv_term, proj_term)


def blocks_for_scatter(term, n_blk, n_dp):
    rows, cols = term.shape
    return (
        term.astype(jnp.bfloat16)
        .reshape(n_blk, rows // n_blk, n_dp, cols // n_dp)
        .transpose(2, 0, 1, 3)
        .reshape(n_dp, n_blk, (rows // n_blk) * (cols // n_dp))
    )


def local(
    audio_frames, conv_weight, proj_weight, text_embed, pair_langs, log_scale, lang_bias, log_var
):
    frames = audio_frames[0]
    text_rows = text_embed[0]
    pair_ids = pair_langs[0]
    local_pairs = frames.shape[0]
    n_blk = lax.axis_size("blk")
    n_dp = lax.axis_size("dp")
    emb = proj_weight.shape[1]
    classes = jnp.arange(log_scale.shape[0], dtype=jnp.int32)
    onehot = (pair_ids[:, None] == classes[None, :]).astype(jnp.float32)
    local_counts = jnp.sum(onehot, axis=0)
    stacked, preact, pooled, audio_unit, audio_len = encode(frames, conv_weight, proj_weight)
    audio_bf = audio_unit.astype(jnp.bfloat16)
    text_unit, text_len = normalize_text(text_rows)
    text_bf = text_unit.astype(jnp.bfloat16)
    id_cols = jnp.broadcast_to(pair_ids.astype(jnp.bfloat16)[:, None], (local_pairs, 128))
    packet = jnp.concatenate([audio_bf, text_bf, id_cols], axis=1)
    packet, local_counts = lax.optimization_barrier((packet, local_counts))
    gathered = lax.all_gather(packet, "blk", axis=0, tiled=True)
    counts = lax.psum(local_counts, ("blk", "dp"))
    all_audio = gathered[:, :emb]
    all_text = gathered[:, emb : 2 * emb]
    all_ids = gathered[:, 2 * emb].astype(jnp.int32)
    weight_table = jnp.exp(-log_var) / jnp.maximum(counts, 1.0)
    scale_table = jnp.exp(log_scale)
    all_onehot = (all_ids[:, None] == classes[None, :]).astype(jnp.float32)
    pair_scale = jnp.sum(all_onehot * scale_table[None, :], axis=1)
    pair_bias = jnp.sum(all_onehot * lang_bias[None, :], axis=1)
    pair_weight = jnp.sum(all_onehot * weight_table[None, :], axis=1)
    logits = (
        pair_scale[:, None]
        * lax.dot_general(
            all_audio, all_text, (((1,), (1,)), ((), ())), preferred_element_type=jnp.float32
        )
        + pair_bias[:, None]
    )
    row_max = jnp.max(logits, axis=1)
    row_lse = row_max + jnp.log(jnp.sum(jnp.exp(logits - row_max[:, None]), axis=1))
    col_max = jnp.max(logits, axis=0)
    col_lse = col_max + jnp.log(jnp.sum(jnp.exp(logits - col_max[None, :]), axis=0))
    positive = jnp.diagonal(logits)
    pair_loss = 0.5 * (row_lse + col_lse) - positive
    index = jnp.arange(logits.shape[0], dtype=jnp.int32)
    on_diagonal = index[:, None] == index[None, :]
    score_grad = 0.5 * (
        pair_weight[:, None] * jnp.exp(logits - row_lse[:, None])
        + pair_weight[None, :] * jnp.exp(logits - col_lse[None, :])
    )
    score_grad = score_grad - jnp.where(on_diagonal, pair_weight[:, None], 0.0)
    scale_terms = jnp.sum(score_grad * (logits - pair_bias[:, None]), axis=1)
    weighted = (score_grad * pair_scale[:, None]).astype(jnp.bfloat16)
    offset = lax.axis_index("blk") * local_pairs
    own_rows = lax.dynamic_slice_in_dim(weighted, offset, local_pairs, 0)
    own_cols = lax.dynamic_slice_in_dim(weighted, offset, local_pairs, 1)
    grad_audio = jnp.dot(own_rows, all_text, preferred_element_type=jnp.float32)
    grad_text = lax.dot_general(
        own_cols, all_audio, (((0,), (0,)), ((), ())), preferred_element_type=jnp.float32
    )
    text_grad = (
        grad_text - text_unit * jnp.sum(text_unit * grad_text, axis=1, keepdims=True)
    ) / text_len
    batch_sums = jnp.stack(
        [
            jnp.sum(all_onehot * pair_loss[:, None], axis=0),
            jnp.sum(all_onehot * scale_terms[:, None], axis=0),
        ]
    )
    conv_term, proj_term = encode_back(
        stacked, preact, pooled, audio_unit, audio_len, grad_audio, proj_weight
    )
    buf = jnp.concatenate(
        [blocks_for_scatter(conv_term, n_blk, n_dp), blocks_for_scatter(proj_term, n_blk, n_dp)],
        axis=2,
    )
    buf, batch_sums = lax.optimization_barrier((buf, batch_sums))
    stage = lax.psum_scatter(buf, "dp", scatter_dimension=0, tiled=True)
    stage = lax.psum_scatter(stage.reshape(n_blk, -1), "blk", scatter_dimension=0, tiled=True)
    loss_sum, scale_grad = lax.psum(batch_sums, "dp")
    conv_rows = conv_term.shape[0] // n_blk
    conv_cols = conv_term.shape[1] // n_dp
    conv_size = conv_rows * conv_cols
    conv_grad = stage[0, :conv_size].reshape(conv_rows, conv_cols).astype(jnp.float32)
    proj_grad = (
        stage[0, conv_size:]
        .reshape(proj_term.shape[0] // n_blk, proj_term.shape[1] // n_dp)
        .astype(jnp.float32)
    )
    var_weight = jnp.exp(-log_var)
    lang_mean = loss_sum / jnp.maximum(counts, 1.0)
    loss = jnp.sum(var_weight * lang_mean + log_var)
    var_grad = 1.0 - var_weight * lang_mean
    return (loss, scale_grad, var_grad, conv_grad, proj_grad, text_grad[None])


def solution(mesh):
    return jax.shard_map(
        local,
        mesh=mesh,
        in_specs=(
            P("dp", "blk", None, None),
            P(),
            P(),
            P("dp", "blk", None),
            P("dp", "blk"),
            P(),
            P(),
            P(),
        ),
        out_specs=(P(), P(), P(), P("blk", "dp"), P("blk", "dp"), P("dp", "blk", None)),
        check_vma=False,
    )
```

```python
import jax
import jax.numpy as jnp
from jax import lax
from jax.sharding import PartitionSpec as P

epsilon = 1e-06


def stack_taps(frames):
    clips, steps_count, channels = frames.shape
    blank = jnp.zeros_like(frames[:, :1])
    before = jnp.concatenate([blank, frames[:, :-1]], axis=1)
    after = jnp.concatenate([frames[:, 1:], blank], axis=1)
    return jnp.concatenate([before, frames, after], axis=2).reshape(
        clips * steps_count, 3 * channels
    )


def encode(frames, conv_weight, proj_weight):
    clips, steps_count, channels = frames.shape
    stacked = stack_taps(frames)
    preact = jnp.dot(stacked, conv_weight, preferred_element_type=jnp.float32)
    pooled = jnp.mean(jax.nn.gelu(preact).reshape(clips, steps_count, -1), axis=1).astype(
        jnp.bfloat16
    )
    embedding = jnp.dot(pooled, proj_weight, preferred_element_type=jnp.float32)
    audio_len = jnp.sqrt(jnp.sum(embedding * embedding, axis=-1, keepdims=True) + epsilon)
    return (stacked, preact, pooled, embedding / audio_len, audio_len)


def normalize_text(text_rows):
    text_float = text_rows.astype(jnp.float32)
    text_len = jnp.sqrt(jnp.sum(text_float * text_float, axis=-1, keepdims=True) + epsilon)
    return (text_float / text_len, text_len)


def encode_back(stacked, preact, pooled, audio_unit, audio_len, grad_audio, proj_weight):
    clips = pooled.shape[0]
    steps_count = preact.shape[0] // clips
    radial = jnp.sum(audio_unit * grad_audio, axis=-1, keepdims=True)
    grad_embed = ((grad_audio - audio_unit * radial) / audio_len).astype(jnp.bfloat16)
    proj_term_t = lax.dot_general(
        grad_embed, pooled, (((0,), (0,)), ((), ())), preferred_element_type=jnp.float32
    )
    grad_pooled = (
        lax.dot_general(
            grad_embed, proj_weight, (((1,), (1,)), ((), ())), preferred_element_type=jnp.float32
        )
        / steps_count
    )
    grad_act = jnp.broadcast_to(
        grad_pooled[:, None, :], (clips, steps_count, grad_pooled.shape[1])
    ).reshape(clips * steps_count, -1)
    grad_pre = jax.vjp(jax.nn.gelu, preact)[1](grad_act)[0].astype(jnp.bfloat16)
    conv_term_t = lax.dot_general(
        grad_pre, stacked, (((0,), (0,)), ((), ())), preferred_element_type=jnp.float32
    )
    return (conv_term_t, proj_term_t)


def scatter_buffer(conv_term_t, proj_term_t, n_blk, n_dp):
    width = conv_term_t.shape[1]
    conv_part = conv_term_t.astype(jnp.bfloat16).reshape(n_dp, -1, width)
    p_cols, p_rows = proj_term_t.shape
    per_block = (p_cols // n_dp) * (p_rows // n_blk)
    seg = width // n_blk
    pad_rows = -(-per_block // seg)
    pad_rows = -(-pad_rows // 16) * 16
    proj_part = (
        proj_term_t.astype(jnp.bfloat16)
        .reshape(n_dp, p_cols // n_dp, n_blk, p_rows // n_blk)
        .transpose(0, 2, 1, 3)
        .reshape(n_dp, n_blk, per_block)
    )
    proj_part = jnp.pad(proj_part, ((0, 0), (0, 0), (0, pad_rows * seg - per_block)))
    proj_part = (
        proj_part.reshape(n_dp, n_blk, pad_rows, seg).transpose(0, 2, 1, 3).reshape(n_dp, pad_rows, width)
    )
    return jnp.concatenate([conv_part, proj_part], axis=1), per_block


def local(
    audio_frames, conv_weight, proj_weight, text_embed, pair_langs, log_scale, lang_bias, log_var
):
    frames = audio_frames[0]
    text_rows = text_embed[0]
    pair_ids = pair_langs[0]
    local_pairs = frames.shape[0]
    n_blk = lax.axis_size("blk")
    n_dp = lax.axis_size("dp")
    emb = proj_weight.shape[1]
    classes = jnp.arange(log_scale.shape[0], dtype=jnp.int32)
    onehot = (pair_ids[:, None] == classes[None, :]).astype(jnp.float32)
    local_counts = jnp.sum(onehot, axis=0)
    stacked, preact, pooled, audio_unit, audio_len = encode(frames, conv_weight, proj_weight)
    audio_bf = audio_unit.astype(jnp.bfloat16)
    text_unit, text_len = normalize_text(text_rows)
    text_bf = text_unit.astype(jnp.bfloat16)
    id_cols = jnp.broadcast_to(pair_ids.astype(jnp.bfloat16)[:, None], (local_pairs, 128))
    packet = jnp.concatenate([audio_bf, text_bf, id_cols], axis=1)
    packet, local_counts = lax.optimization_barrier((packet, local_counts))
    gathered = lax.all_gather(packet, "blk", axis=0, tiled=True)
    counts = lax.psum(local_counts, ("blk", "dp"))
    all_audio = gathered[:, :emb]
    all_text = gathered[:, emb : 2 * emb]
    all_ids = gathered[:, 2 * emb].astype(jnp.int32)
    weight_table = jnp.exp(-log_var) / jnp.maximum(counts, 1.0)
    scale_table = jnp.exp(log_scale)
    all_onehot = (all_ids[:, None] == classes[None, :]).astype(jnp.float32)
    pair_scale = jnp.sum(all_onehot * scale_table[None, :], axis=1)
    pair_bias = jnp.sum(all_onehot * lang_bias[None, :], axis=1)
    pair_weight = jnp.sum(all_onehot * weight_table[None, :], axis=1)
    logits = (
        pair_scale[:, None]
        * lax.dot_general(
            all_audio, all_text, (((1,), (1,)), ((), ())), preferred_element_type=jnp.float32
        )
        + pair_bias[:, None]
    )
    row_max = jnp.max(logits, axis=1)
    row_lse = row_max + jnp.log(jnp.sum(jnp.exp(logits - row_max[:, None]), axis=1))
    col_max = jnp.max(logits, axis=0)
    col_lse = col_max + jnp.log(jnp.sum(jnp.exp(logits - col_max[None, :]), axis=0))
    index = jnp.arange(logits.shape[0], dtype=jnp.int32)
    on_diagonal = index[:, None] == index[None, :]
    positive = jnp.sum(jnp.where(on_diagonal, logits, 0.0), axis=1)
    pair_loss = 0.5 * (row_lse + col_lse) - positive
    score_grad = 0.5 * (
        pair_weight[:, None] * jnp.exp(logits - row_lse[:, None])
        + pair_weight[None, :] * jnp.exp(logits - col_lse[None, :])
    )
    score_grad = score_grad - jnp.where(on_diagonal, pair_weight[:, None], 0.0)
    scale_terms = jnp.sum(score_grad * (logits - pair_bias[:, None]), axis=1)
    weighted = (score_grad * pair_scale[:, None]).astype(jnp.bfloat16)
    offset = lax.axis_index("blk") * local_pairs
    own_rows = lax.dynamic_slice_in_dim(weighted, offset, local_pairs, 0)
    own_cols = lax.dynamic_slice_in_dim(weighted, offset, local_pairs, 1)
    grad_audio = jnp.dot(own_rows, all_text, preferred_element_type=jnp.float32)
    grad_text = lax.dot_general(
        own_cols, all_audio, (((0,), (0,)), ((), ())), preferred_element_type=jnp.float32
    )
    text_grad = (
        grad_text - text_unit * jnp.sum(text_unit * grad_text, axis=1, keepdims=True)
    ) / text_len
    batch_sums = jnp.stack(
        [
            jnp.sum(all_onehot * pair_loss[:, None], axis=0),
            jnp.sum(all_onehot * scale_terms[:, None], axis=0),
        ]
    )
    conv_term_t, proj_term_t = encode_back(
        stacked, preact, pooled, audio_unit, audio_len, grad_audio, proj_weight
    )
    buf, per_block = scatter_buffer(conv_term_t, proj_term_t, n_blk, n_dp)
    buf, batch_sums = lax.optimization_barrier((buf, batch_sums))
    stage = lax.psum_scatter(buf, "dp", scatter_dimension=0, tiled=True)
    stage = lax.psum_scatter(stage[0], "blk", scatter_dimension=1, tiled=True)
    loss_sum, scale_grad = lax.psum(batch_sums, "dp")
    conv_cols = conv_term_t.shape[0] // n_dp
    conv_grad = stage[:conv_cols].T.astype(jnp.float32)
    proj_grad = (
        stage[conv_cols:]
        .reshape(-1)[:per_block]
        .reshape(proj_term_t.shape[0] // n_dp, proj_term_t.shape[1] // n_blk)
        .T.astype(jnp.float32)
    )
    var_weight = jnp.exp(-log_var)
    lang_mean = loss_sum / jnp.maximum(counts, 1.0)
    loss = jnp.sum(var_weight * lang_mean + log_var)
    var_grad = 1.0 - var_weight * lang_mean
    return (loss, scale_grad, var_grad, conv_grad, proj_grad, text_grad[None])


def solution(mesh):
    return jax.shard_map(
        local,
        mesh=mesh,
        in_specs=(
            P("dp", "blk", None, None),
            P(),
            P(),
            P("dp", "blk", None),
            P("dp", "blk"),
            P(),
            P(),
            P(),
        ),
        out_specs=(P(), P(), P(), P("blk", "dp"), P("blk", "dp"), P("dp", "blk", None)),
        check_vma=False,
    )
```

```python
import jax
import jax.numpy as jnp
from jax import lax
from jax.sharding import PartitionSpec as P

epsilon = 1e-06


def stack_taps(frames):
    clips, steps_count, channels = frames.shape
    blank = jnp.zeros_like(frames[:, :1])
    before = jnp.concatenate([blank, frames[:, :-1]], axis=1)
    after = jnp.concatenate([frames[:, 1:], blank], axis=1)
    return jnp.concatenate([before, frames, after], axis=2).reshape(
        clips * steps_count, 3 * channels
    )


def encode(frames, conv_weight, proj_weight):
    clips, steps_count, channels = frames.shape
    stacked = stack_taps(frames)
    preact = jnp.dot(stacked, conv_weight, preferred_element_type=jnp.float32)
    pooled = jnp.mean(jax.nn.gelu(preact).reshape(clips, steps_count, -1), axis=1).astype(
        jnp.bfloat16
    )
    embedding = jnp.dot(pooled, proj_weight, preferred_element_type=jnp.float32)
    audio_len = jnp.sqrt(jnp.sum(embedding * embedding, axis=-1, keepdims=True) + epsilon)
    return (stacked, preact, pooled, embedding / audio_len, audio_len)


def normalize_text(text_rows):
    text_float = text_rows.astype(jnp.float32)
    text_len = jnp.sqrt(jnp.sum(text_float * text_float, axis=-1, keepdims=True) + epsilon)
    return (text_float / text_len, text_len)


def encode_back(stacked, preact, pooled, audio_unit, audio_len, grad_audio, proj_weight, n_dp):
    clips = pooled.shape[0]
    steps_count = preact.shape[0] // clips
    radial = jnp.sum(audio_unit * grad_audio, axis=-1, keepdims=True)
    grad_embed = ((grad_audio - audio_unit * radial) / audio_len).astype(jnp.bfloat16)
    emb = grad_embed.shape[1]
    width = preact.shape[1]
    padded = jnp.pad(
        grad_embed.reshape(clips, n_dp, emb // n_dp),
        ((0, 0), (0, 0), (0, (width - emb) // n_dp)),
    ).reshape(clips, width)
    proj_term = lax.dot_general(
        pooled, padded, (((0,), (0,)), ((), ())), preferred_element_type=jnp.float32
    )
    grad_pooled = (
        lax.dot_general(
            grad_embed, proj_weight, (((1,), (1,)), ((), ())), preferred_element_type=jnp.float32
        )
        / steps_count
    )
    grad_act = jnp.broadcast_to(
        grad_pooled[:, None, :], (clips, steps_count, grad_pooled.shape[1])
    ).reshape(clips * steps_count, -1)
    grad_pre = jax.vjp(jax.nn.gelu, preact)[1](grad_act)[0].astype(jnp.bfloat16)
    conv_term = lax.dot_general(
        stacked, grad_pre, (((0,), (0,)), ((), ())), preferred_element_type=jnp.float32
    )
    return (conv_term, proj_term)


def local(
    audio_frames, conv_weight, proj_weight, text_embed, pair_langs, log_scale, lang_bias, log_var
):
    frames = audio_frames[0]
    text_rows = text_embed[0]
    pair_ids = pair_langs[0]
    local_pairs = frames.shape[0]
    n_blk = lax.axis_size("blk")
    n_dp = lax.axis_size("dp")
    emb = proj_weight.shape[1]
    classes = jnp.arange(log_scale.shape[0], dtype=jnp.int32)
    onehot = (pair_ids[:, None] == classes[None, :]).astype(jnp.float32)
    local_counts = jnp.sum(onehot, axis=0)
    stacked, preact, pooled, audio_unit, audio_len = encode(frames, conv_weight, proj_weight)
    audio_bf = audio_unit.astype(jnp.bfloat16)
    text_unit, text_len = normalize_text(text_rows)
    text_bf = text_unit.astype(jnp.bfloat16)
    id_cols = jnp.broadcast_to(pair_ids.astype(jnp.bfloat16)[:, None], (local_pairs, 128))
    packet = jnp.concatenate([audio_bf, text_bf, id_cols], axis=1)
    packet, local_counts = lax.optimization_barrier((packet, local_counts))
    gathered = lax.all_gather(packet, "blk", axis=0, tiled=True)
    counts = lax.psum(local_counts, ("blk", "dp"))
    all_audio = gathered[:, :emb]
    all_text = gathered[:, emb : 2 * emb]
    all_ids = gathered[:, 2 * emb].astype(jnp.int32)
    weight_table = jnp.exp(-log_var) / jnp.maximum(counts, 1.0)
    scale_table = jnp.exp(log_scale)
    all_onehot = (all_ids[:, None] == classes[None, :]).astype(jnp.float32)
    pair_scale = jnp.sum(all_onehot * scale_table[None, :], axis=1)
    pair_bias = jnp.sum(all_onehot * lang_bias[None, :], axis=1)
    pair_weight = jnp.sum(all_onehot * weight_table[None, :], axis=1)
    logits = (
        pair_scale[:, None]
        * lax.dot_general(
            all_audio, all_text, (((1,), (1,)), ((), ())), preferred_element_type=jnp.float32
        )
        + pair_bias[:, None]
    )
    row_max = jnp.max(logits, axis=1)
    row_lse = row_max + jnp.log(jnp.sum(jnp.exp(logits - row_max[:, None]), axis=1))
    col_max = jnp.max(logits, axis=0)
    col_lse = col_max + jnp.log(jnp.sum(jnp.exp(logits - col_max[None, :]), axis=0))
    index = jnp.arange(logits.shape[0], dtype=jnp.int32)
    on_diagonal = index[:, None] == index[None, :]
    positive = jnp.sum(jnp.where(on_diagonal, logits, 0.0), axis=1)
    pair_loss = 0.5 * (row_lse + col_lse) - positive
    score_grad = 0.5 * (
        pair_weight[:, None] * jnp.exp(logits - row_lse[:, None])
        + pair_weight[None, :] * jnp.exp(logits - col_lse[None, :])
    )
    score_grad = score_grad - jnp.where(on_diagonal, pair_weight[:, None], 0.0)
    scale_terms = jnp.sum(score_grad * (logits - pair_bias[:, None]), axis=1)
    weighted = (score_grad * pair_scale[:, None]).astype(jnp.bfloat16)
    offset = lax.axis_index("blk") * local_pairs
    own_rows = lax.dynamic_slice_in_dim(weighted, offset, local_pairs, 0)
    own_cols = lax.dynamic_slice_in_dim(weighted, offset, local_pairs, 1)
    grad_audio = jnp.dot(own_rows, all_text, preferred_element_type=jnp.float32)
    grad_text = lax.dot_general(
        own_cols, all_audio, (((0,), (0,)), ((), ())), preferred_element_type=jnp.float32
    )
    text_grad = (
        grad_text - text_unit * jnp.sum(text_unit * grad_text, axis=1, keepdims=True)
    ) / text_len
    batch_sums = jnp.stack(
        [
            jnp.sum(all_onehot * pair_loss[:, None], axis=0),
            jnp.sum(all_onehot * scale_terms[:, None], axis=0),
        ]
    )
    conv_term, proj_term = encode_back(
        stacked, preact, pooled, audio_unit, audio_len, grad_audio, proj_weight, n_dp
    )
    conv_rows = conv_term.shape[0] // n_blk
    proj_rows = proj_term.shape[0] // n_blk
    buf = jnp.concatenate(
        [
            conv_term.astype(jnp.bfloat16).reshape(n_blk, conv_rows, -1),
            proj_term.astype(jnp.bfloat16).reshape(n_blk, proj_rows, -1),
        ],
        axis=1,
    )
    buf, batch_sums = lax.optimization_barrier((buf, batch_sums))
    stage = lax.psum_scatter(buf, "blk", scatter_dimension=0, tiled=True)
    stage = lax.psum_scatter(stage[0], "dp", scatter_dimension=1, tiled=True)
    loss_sum, scale_grad = lax.psum(batch_sums, "dp")
    conv_grad = stage[:conv_rows].astype(jnp.float32)
    proj_grad = stage[conv_rows:, : emb // n_dp].astype(jnp.float32)
    var_weight = jnp.exp(-log_var)
    lang_mean = loss_sum / jnp.maximum(counts, 1.0)
    loss = jnp.sum(var_weight * lang_mean + log_var)
    var_grad = 1.0 - var_weight * lang_mean
    return (loss, scale_grad, var_grad, conv_grad, proj_grad, text_grad[None])


def solution(mesh):
    return jax.shard_map(
        local,
        mesh=mesh,
        in_specs=(
            P("dp", "blk", None, None),
            P(),
            P(),
            P("dp", "blk", None),
            P("dp", "blk"),
            P(),
            P(),
            P(),
        ),
        out_specs=(P(), P(), P(), P("blk", "dp"), P("blk", "dp"), P("dp", "blk", None)),
        check_vma=False,
    )
```

```python
import jax
import jax.numpy as jnp
from jax import lax
from jax.sharding import PartitionSpec as P

epsilon = 1e-06


def stack_taps(frames):
    clips, steps_count, channels = frames.shape
    blank = jnp.zeros_like(frames[:, :1])
    before = jnp.concatenate([blank, frames[:, :-1]], axis=1)
    after = jnp.concatenate([frames[:, 1:], blank], axis=1)
    return jnp.concatenate([before, frames, after], axis=2).reshape(
        clips * steps_count, 3 * channels
    )


def encode(frames, conv_weight, proj_weight):
    clips, steps_count, channels = frames.shape
    stacked = stack_taps(frames)
    preact = jnp.dot(stacked, conv_weight, preferred_element_type=jnp.float32)
    pooled = jnp.mean(jax.nn.gelu(preact).reshape(clips, steps_count, -1), axis=1).astype(
        jnp.bfloat16
    )
    embedding = jnp.dot(pooled, proj_weight, preferred_element_type=jnp.float32)
    audio_len = jnp.sqrt(jnp.sum(embedding * embedding, axis=-1, keepdims=True) + epsilon)
    return (stacked, preact, pooled, embedding / audio_len, audio_len)


def normalize_text(text_rows):
    text_float = text_rows.astype(jnp.float32)
    text_len = jnp.sqrt(jnp.sum(text_float * text_float, axis=-1, keepdims=True) + epsilon)
    return (text_float / text_len, text_len)


def encode_back(stacked, preact, pooled, audio_unit, audio_len, grad_audio, proj_weight):
    clips = pooled.shape[0]
    steps_count = preact.shape[0] // clips
    radial = jnp.sum(audio_unit * grad_audio, axis=-1, keepdims=True)
    grad_embed = ((grad_audio - audio_unit * radial) / audio_len).astype(jnp.bfloat16)
    proj_term_t = lax.dot_general(
        grad_embed, pooled, (((0,), (0,)), ((), ())), preferred_element_type=jnp.float32
    )
    grad_pooled = (
        lax.dot_general(
            grad_embed, proj_weight, (((1,), (1,)), ((), ())), preferred_element_type=jnp.float32
        )
        / steps_count
    )
    grad_act = jnp.broadcast_to(
        grad_pooled[:, None, :], (clips, steps_count, grad_pooled.shape[1])
    ).reshape(clips * steps_count, -1)
    grad_pre = jax.vjp(jax.nn.gelu, preact)[1](grad_act)[0].astype(jnp.bfloat16)
    conv_term_t = lax.dot_general(
        grad_pre, stacked, (((0,), (0,)), ((), ())), preferred_element_type=jnp.float32
    )
    return (conv_term_t, proj_term_t)


def scatter_buffer(conv_term_t, proj_term_t, n_blk, n_dp):
    width = conv_term_t.shape[1]
    conv_part = conv_term_t.astype(jnp.bfloat16).reshape(n_dp, -1, width)
    p_cols, p_rows = proj_term_t.shape
    per_block = (p_cols // n_dp) * (p_rows // n_blk)
    seg = width // n_blk
    pad_rows = -(-per_block // seg)
    pad_rows = -(-pad_rows // 16) * 16
    proj_part = (
        proj_term_t.astype(jnp.bfloat16)
        .reshape(n_dp, p_cols // n_dp, n_blk, p_rows // n_blk)
        .transpose(0, 2, 1, 3)
        .reshape(n_dp, n_blk, per_block)
    )
    proj_part = jnp.pad(proj_part, ((0, 0), (0, 0), (0, pad_rows * seg - per_block)))
    proj_part = (
        proj_part.reshape(n_dp, n_blk, pad_rows, seg).transpose(0, 2, 1, 3).reshape(n_dp, pad_rows, width)
    )
    return jnp.concatenate([conv_part, proj_part], axis=1), per_block


def halving_scatter(rows, split, n_blk):
    me = lax.axis_index("blk")
    parts = [rows[:split], rows[split:]]
    parts = [p.reshape(p.shape[0], n_blk, -1).astype(jnp.float32) for p in parts]
    bit = 1
    while bit < n_blk:
        mine = (me // bit) % 2
        pairs = [(i, i ^ bit) for i in range(n_blk)]
        kept = []
        for p in parts:
            grouped = p.reshape(p.shape[0], p.shape[1] // 2, 2, p.shape[2])
            keep = lax.dynamic_index_in_dim(grouped, mine, axis=2, keepdims=False)
            send = lax.dynamic_index_in_dim(grouped, 1 - mine, axis=2, keepdims=False)
            got = lax.ppermute(send.astype(jnp.bfloat16), "blk", pairs)
            kept.append(keep + got.astype(jnp.float32))
        parts = kept
        bit *= 2
    return [p[:, 0, :] for p in parts]


def local(
    audio_frames, conv_weight, proj_weight, text_embed, pair_langs, log_scale, lang_bias, log_var
):
    frames = audio_frames[0]
    text_rows = text_embed[0]
    pair_ids = pair_langs[0]
    local_pairs = frames.shape[0]
    n_blk = lax.axis_size("blk")
    n_dp = lax.axis_size("dp")
    emb = proj_weight.shape[1]
    classes = jnp.arange(log_scale.shape[0], dtype=jnp.int32)
    onehot = (pair_ids[:, None] == classes[None, :]).astype(jnp.float32)
    local_counts = jnp.sum(onehot, axis=0)
    stacked, preact, pooled, audio_unit, audio_len = encode(frames, conv_weight, proj_weight)
    audio_bf = audio_unit.astype(jnp.bfloat16)
    text_unit, text_len = normalize_text(text_rows)
    text_bf = text_unit.astype(jnp.bfloat16)
    id_cols = jnp.broadcast_to(pair_ids.astype(jnp.bfloat16)[:, None], (local_pairs, 128))
    packet = jnp.concatenate([audio_bf, text_bf, id_cols], axis=1)
    packet, local_counts = lax.optimization_barrier((packet, local_counts))
    gathered = lax.all_gather(packet, "blk", axis=0, tiled=True)
    counts = lax.psum(local_counts, ("blk", "dp"))
    all_audio = gathered[:, :emb]
    all_text = gathered[:, emb : 2 * emb]
    all_ids = gathered[:, 2 * emb].astype(jnp.int32)
    weight_table = jnp.exp(-log_var) / jnp.maximum(counts, 1.0)
    scale_table = jnp.exp(log_scale)
    all_onehot = (all_ids[:, None] == classes[None, :]).astype(jnp.float32)
    pair_scale = jnp.sum(all_onehot * scale_table[None, :], axis=1)
    pair_bias = jnp.sum(all_onehot * lang_bias[None, :], axis=1)
    pair_weight = jnp.sum(all_onehot * weight_table[None, :], axis=1)
    logits = (
        pair_scale[:, None]
        * lax.dot_general(
            all_audio, all_text, (((1,), (1,)), ((), ())), preferred_element_type=jnp.float32
        )
        + pair_bias[:, None]
    )
    row_max = jnp.max(logits, axis=1)
    row_lse = row_max + jnp.log(jnp.sum(jnp.exp(logits - row_max[:, None]), axis=1))
    col_max = jnp.max(logits, axis=0)
    col_lse = col_max + jnp.log(jnp.sum(jnp.exp(logits - col_max[None, :]), axis=0))
    index = jnp.arange(logits.shape[0], dtype=jnp.int32)
    on_diagonal = index[:, None] == index[None, :]
    positive = jnp.sum(jnp.where(on_diagonal, logits, 0.0), axis=1)
    pair_loss = 0.5 * (row_lse + col_lse) - positive
    score_grad = 0.5 * (
        pair_weight[:, None] * jnp.exp(logits - row_lse[:, None])
        + pair_weight[None, :] * jnp.exp(logits - col_lse[None, :])
    )
    score_grad = score_grad - jnp.where(on_diagonal, pair_weight[:, None], 0.0)
    scale_terms = jnp.sum(score_grad * (logits - pair_bias[:, None]), axis=1)
    weighted = (score_grad * pair_scale[:, None]).astype(jnp.bfloat16)
    offset = lax.axis_index("blk") * local_pairs
    own_rows = lax.dynamic_slice_in_dim(weighted, offset, local_pairs, 0)
    own_cols = lax.dynamic_slice_in_dim(weighted, offset, local_pairs, 1)
    grad_audio = jnp.dot(own_rows, all_text, preferred_element_type=jnp.float32)
    grad_text = lax.dot_general(
        own_cols, all_audio, (((0,), (0,)), ((), ())), preferred_element_type=jnp.float32
    )
    text_grad = (
        grad_text - text_unit * jnp.sum(text_unit * grad_text, axis=1, keepdims=True)
    ) / text_len
    batch_sums = jnp.stack(
        [
            jnp.sum(all_onehot * pair_loss[:, None], axis=0),
            jnp.sum(all_onehot * scale_terms[:, None], axis=0),
        ]
    )
    conv_term_t, proj_term_t = encode_back(
        stacked, preact, pooled, audio_unit, audio_len, grad_audio, proj_weight
    )
    buf, per_block = scatter_buffer(conv_term_t, proj_term_t, n_blk, n_dp)
    buf, batch_sums = lax.optimization_barrier((buf, batch_sums))
    stage = lax.psum_scatter(buf, "dp", scatter_dimension=0, tiled=True)
    loss_sum, scale_grad = lax.psum(batch_sums, "dp")
    conv_cols = conv_term_t.shape[0] // n_dp
    conv_part, proj_part = halving_scatter(stage[0], conv_cols, n_blk)
    conv_grad = conv_part.T
    proj_grad = (
        proj_part.reshape(-1)[:per_block]
        .reshape(proj_term_t.shape[0] // n_dp, proj_term_t.shape[1] // n_blk)
        .T
    )
    var_weight = jnp.exp(-log_var)
    lang_mean = loss_sum / jnp.maximum(counts, 1.0)
    loss = jnp.sum(var_weight * lang_mean + log_var)
    var_grad = 1.0 - var_weight * lang_mean
    return (loss, scale_grad, var_grad, conv_grad, proj_grad, text_grad[None])


def solution(mesh):
    return jax.shard_map(
        local,
        mesh=mesh,
        in_specs=(
            P("dp", "blk", None, None),
            P(),
            P(),
            P("dp", "blk", None),
            P("dp", "blk"),
            P(),
            P(),
            P(),
        ),
        out_specs=(P(), P(), P(), P("blk", "dp"), P("blk", "dp"), P("dp", "blk", None)),
        check_vma=False,
    )
```

```python
import jax
import jax.numpy as jnp
from jax import lax
from jax.sharding import PartitionSpec as P

epsilon = 1e-06


def stack_taps(frames):
    clips, steps_count, channels = frames.shape
    blank = jnp.zeros_like(frames[:, :1])
    before = jnp.concatenate([blank, frames[:, :-1]], axis=1)
    after = jnp.concatenate([frames[:, 1:], blank], axis=1)
    return jnp.concatenate([before, frames, after], axis=2).reshape(
        clips * steps_count, 3 * channels
    )


def encode(frames, conv_weight, proj_weight):
    clips, steps_count, channels = frames.shape
    stacked = stack_taps(frames)
    preact = jnp.dot(stacked, conv_weight, preferred_element_type=jnp.float32)
    pooled = jnp.mean(jax.nn.gelu(preact).reshape(clips, steps_count, -1), axis=1).astype(
        jnp.bfloat16
    )
    embedding = jnp.dot(pooled, proj_weight, preferred_element_type=jnp.float32)
    audio_len = jnp.sqrt(jnp.sum(embedding * embedding, axis=-1, keepdims=True) + epsilon)
    return (stacked, preact, pooled, embedding / audio_len, audio_len)


def normalize_text(text_rows):
    text_float = text_rows.astype(jnp.float32)
    text_len = jnp.sqrt(jnp.sum(text_float * text_float, axis=-1, keepdims=True) + epsilon)
    return (text_float / text_len, text_len)


def encode_back(stacked, preact, pooled, audio_unit, audio_len, grad_audio, proj_weight):
    clips = pooled.shape[0]
    steps_count = preact.shape[0] // clips
    radial = jnp.sum(audio_unit * grad_audio, axis=-1, keepdims=True)
    grad_embed = ((grad_audio - audio_unit * radial) / audio_len).astype(jnp.bfloat16)
    proj_term_t = lax.dot_general(
        grad_embed, pooled, (((0,), (0,)), ((), ())), preferred_element_type=jnp.float32
    )
    grad_pooled = (
        lax.dot_general(
            grad_embed, proj_weight, (((1,), (1,)), ((), ())), preferred_element_type=jnp.float32
        )
        / steps_count
    )
    grad_act = jnp.broadcast_to(
        grad_pooled[:, None, :], (clips, steps_count, grad_pooled.shape[1])
    ).reshape(clips * steps_count, -1)
    grad_pre = jax.vjp(jax.nn.gelu, preact)[1](grad_act)[0].astype(jnp.bfloat16)
    conv_term_t = lax.dot_general(
        grad_pre, stacked, (((0,), (0,)), ((), ())), preferred_element_type=jnp.float32
    )
    return (conv_term_t, proj_term_t)


def scatter_buffer(conv_term_t, proj_term_t, n_dp):
    return jnp.concatenate(
        [
            conv_term_t.astype(jnp.bfloat16).reshape(n_dp, -1),
            proj_term_t.astype(jnp.bfloat16).reshape(n_dp, -1),
        ],
        axis=1,
    )


def halving_scatter(parts, n_blk):
    me = lax.axis_index("blk")
    parts = [p.reshape(p.shape[0], n_blk, -1).astype(jnp.float32) for p in parts]
    bit = 1
    while bit < n_blk:
        mine = (me // bit) % 2
        pairs = [(i, i ^ bit) for i in range(n_blk)]
        kept = []
        for p in parts:
            grouped = p.reshape(p.shape[0], p.shape[1] // 2, 2, p.shape[2])
            keep = lax.dynamic_index_in_dim(grouped, mine, axis=2, keepdims=False)
            send = lax.dynamic_index_in_dim(grouped, 1 - mine, axis=2, keepdims=False)
            got = lax.ppermute(send.astype(jnp.bfloat16), "blk", pairs)
            kept.append(keep + got.astype(jnp.float32))
        parts = kept
        bit *= 2
    return [p[:, 0, :] for p in parts]


def local(
    audio_frames, conv_weight, proj_weight, text_embed, pair_langs, log_scale, lang_bias, log_var
):
    frames = audio_frames[0]
    text_rows = text_embed[0]
    pair_ids = pair_langs[0]
    local_pairs = frames.shape[0]
    n_blk = lax.axis_size("blk")
    n_dp = lax.axis_size("dp")
    emb = proj_weight.shape[1]
    classes = jnp.arange(log_scale.shape[0], dtype=jnp.int32)
    onehot = (pair_ids[:, None] == classes[None, :]).astype(jnp.float32)
    local_counts = jnp.sum(onehot, axis=0)
    stacked, preact, pooled, audio_unit, audio_len = encode(frames, conv_weight, proj_weight)
    audio_bf = audio_unit.astype(jnp.bfloat16)
    text_unit, text_len = normalize_text(text_rows)
    text_bf = text_unit.astype(jnp.bfloat16)
    id_cols = jnp.broadcast_to(pair_ids.astype(jnp.bfloat16)[:, None], (local_pairs, 128))
    packet = jnp.concatenate([audio_bf, text_bf, id_cols], axis=1)
    packet, local_counts = lax.optimization_barrier((packet, local_counts))
    gathered = lax.all_gather(packet, "blk", axis=0, tiled=True)
    counts = lax.psum(local_counts, ("blk", "dp"))
    all_audio = gathered[:, :emb]
    all_text = gathered[:, emb : 2 * emb]
    all_ids = gathered[:, 2 * emb].astype(jnp.int32)
    weight_table = jnp.exp(-log_var) / jnp.maximum(counts, 1.0)
    scale_table = jnp.exp(log_scale)
    all_onehot = (all_ids[:, None] == classes[None, :]).astype(jnp.float32)
    pair_scale = jnp.sum(all_onehot * scale_table[None, :], axis=1)
    pair_bias = jnp.sum(all_onehot * lang_bias[None, :], axis=1)
    pair_weight = jnp.sum(all_onehot * weight_table[None, :], axis=1)
    logits = (
        pair_scale[:, None]
        * lax.dot_general(
            all_audio, all_text, (((1,), (1,)), ((), ())), preferred_element_type=jnp.float32
        )
        + pair_bias[:, None]
    )
    row_max = jnp.max(logits, axis=1)
    row_lse = row_max + jnp.log(jnp.sum(jnp.exp(logits - row_max[:, None]), axis=1))
    col_max = jnp.max(logits, axis=0)
    col_lse = col_max + jnp.log(jnp.sum(jnp.exp(logits - col_max[None, :]), axis=0))
    index = jnp.arange(logits.shape[0], dtype=jnp.int32)
    on_diagonal = index[:, None] == index[None, :]
    positive = jnp.sum(jnp.where(on_diagonal, logits, 0.0), axis=1)
    pair_loss = 0.5 * (row_lse + col_lse) - positive
    score_grad = 0.5 * (
        pair_weight[:, None] * jnp.exp(logits - row_lse[:, None])
        + pair_weight[None, :] * jnp.exp(logits - col_lse[None, :])
    )
    score_grad = score_grad - jnp.where(on_diagonal, pair_weight[:, None], 0.0)
    scale_terms = jnp.sum(score_grad * (logits - pair_bias[:, None]), axis=1)
    weighted = (score_grad * pair_scale[:, None]).astype(jnp.bfloat16)
    offset = lax.axis_index("blk") * local_pairs
    own_rows = lax.dynamic_slice_in_dim(weighted, offset, local_pairs, 0)
    own_cols = lax.dynamic_slice_in_dim(weighted, offset, local_pairs, 1)
    grad_audio = jnp.dot(own_rows, all_text, preferred_element_type=jnp.float32)
    grad_text = lax.dot_general(
        own_cols, all_audio, (((0,), (0,)), ((), ())), preferred_element_type=jnp.float32
    )
    text_grad = (
        grad_text - text_unit * jnp.sum(text_unit * grad_text, axis=1, keepdims=True)
    ) / text_len
    batch_sums = jnp.stack(
        [
            jnp.sum(all_onehot * pair_loss[:, None], axis=0),
            jnp.sum(all_onehot * scale_terms[:, None], axis=0),
        ]
    )
    conv_term_t, proj_term_t = encode_back(
        stacked, preact, pooled, audio_unit, audio_len, grad_audio, proj_weight
    )
    buf = scatter_buffer(conv_term_t, proj_term_t, n_dp)
    buf, batch_sums = lax.optimization_barrier((buf, batch_sums))
    stage = lax.psum_scatter(buf, "dp", scatter_dimension=0, tiled=True)
    loss_sum, scale_grad = lax.psum(batch_sums, "dp")
    conv_cols = conv_term_t.shape[0] // n_dp
    proj_cols = proj_term_t.shape[0] // n_dp
    conv_size = conv_cols * conv_term_t.shape[1]
    conv_part, proj_part = halving_scatter(
        [
            stage[0, :conv_size].reshape(conv_cols, -1),
            stage[0, conv_size:].reshape(proj_cols, -1),
        ],
        n_blk,
    )
    conv_grad = conv_part.T
    proj_grad = proj_part.T
    var_weight = jnp.exp(-log_var)
    lang_mean = loss_sum / jnp.maximum(counts, 1.0)
    loss = jnp.sum(var_weight * lang_mean + log_var)
    var_grad = 1.0 - var_weight * lang_mean
    return (loss, scale_grad, var_grad, conv_grad, proj_grad, text_grad[None])


def solution(mesh):
    return jax.shard_map(
        local,
        mesh=mesh,
        in_specs=(
            P("dp", "blk", None, None),
            P(),
            P(),
            P("dp", "blk", None),
            P("dp", "blk"),
            P(),
            P(),
            P(),
        ),
        out_specs=(P(), P(), P(), P("blk", "dp"), P("blk", "dp"), P("dp", "blk", None)),
        check_vma=False,
    )
```

```python
import jax
import jax.numpy as jnp
from jax import lax
from jax.sharding import PartitionSpec as P

epsilon = 1e-06


def stack_taps(frames):
    clips, steps_count, channels = frames.shape
    blank = jnp.zeros_like(frames[:, :1])
    before = jnp.concatenate([blank, frames[:, :-1]], axis=1)
    after = jnp.concatenate([frames[:, 1:], blank], axis=1)
    return jnp.concatenate([before, frames, after], axis=2).reshape(
        clips * steps_count, 3 * channels
    )


def encode(frames, conv_weight, proj_weight):
    clips, steps_count, channels = frames.shape
    stacked = stack_taps(frames)
    preact = jnp.dot(stacked, conv_weight, preferred_element_type=jnp.float32)
    pooled = jnp.mean(jax.nn.gelu(preact).reshape(clips, steps_count, -1), axis=1).astype(
        jnp.bfloat16
    )
    embedding = jnp.dot(pooled, proj_weight, preferred_element_type=jnp.float32)
    audio_len = jnp.sqrt(jnp.sum(embedding * embedding, axis=-1, keepdims=True) + epsilon)
    return (stacked, preact, pooled, embedding / audio_len, audio_len)


def normalize_text(text_rows):
    text_float = text_rows.astype(jnp.float32)
    text_len = jnp.sqrt(jnp.sum(text_float * text_float, axis=-1, keepdims=True) + epsilon)
    return (text_float / text_len, text_len)


def encode_back(stacked, preact, pooled, audio_unit, audio_len, grad_audio, proj_weight):
    clips = pooled.shape[0]
    steps_count = preact.shape[0] // clips
    radial = jnp.sum(audio_unit * grad_audio, axis=-1, keepdims=True)
    grad_embed = ((grad_audio - audio_unit * radial) / audio_len).astype(jnp.bfloat16)
    proj_term_t = lax.dot_general(
        grad_embed, pooled, (((0,), (0,)), ((), ())), preferred_element_type=jnp.float32
    )
    grad_pooled = (
        lax.dot_general(
            grad_embed, proj_weight, (((1,), (1,)), ((), ())), preferred_element_type=jnp.float32
        )
        / steps_count
    )
    grad_act = jnp.broadcast_to(
        grad_pooled[:, None, :], (clips, steps_count, grad_pooled.shape[1])
    ).reshape(clips * steps_count, -1)
    grad_pre = jax.vjp(jax.nn.gelu, preact)[1](grad_act)[0].astype(jnp.bfloat16)
    conv_term_t = lax.dot_general(
        grad_pre, stacked, (((0,), (0,)), ((), ())), preferred_element_type=jnp.float32
    )
    return (conv_term_t, proj_term_t)


def scatter_buffer(conv_term_t, proj_term_t, n_blk, n_dp):
    width = conv_term_t.shape[1]
    conv_part = conv_term_t.astype(jnp.bfloat16).reshape(n_dp, -1, width)
    p_cols, p_rows = proj_term_t.shape
    per_block = (p_cols // n_dp) * (p_rows // n_blk)
    seg = width // n_blk
    pad_rows = -(-per_block // seg)
    pad_rows = -(-pad_rows // 16) * 16
    proj_part = (
        proj_term_t.astype(jnp.bfloat16)
        .reshape(n_dp, p_cols // n_dp, n_blk, p_rows // n_blk)
        .transpose(0, 2, 1, 3)
        .reshape(n_dp, n_blk, per_block)
    )
    proj_part = jnp.pad(proj_part, ((0, 0), (0, 0), (0, pad_rows * seg - per_block)))
    proj_part = (
        proj_part.reshape(n_dp, n_blk, pad_rows, seg).transpose(0, 2, 1, 3).reshape(n_dp, pad_rows, width)
    )
    return jnp.concatenate([conv_part, proj_part], axis=1), per_block


def halving_scatter(rows, split, n_blk):
    me = lax.axis_index("blk")
    parts = [rows[:split], rows[split:]]
    parts = [p.reshape(p.shape[0], n_blk, -1).astype(jnp.float32) for p in parts]
    bit = 1
    while bit < n_blk:
        mine = (me // bit) % 2
        pairs = [(i, i ^ bit) for i in range(n_blk)]
        kept = []
        for p in parts:
            grouped = p.reshape(p.shape[0], p.shape[1] // 2, 2, p.shape[2])
            keep = lax.dynamic_index_in_dim(grouped, mine, axis=2, keepdims=False)
            send = lax.dynamic_index_in_dim(grouped, 1 - mine, axis=2, keepdims=False)
            got = lax.ppermute(send.astype(jnp.bfloat16), "blk", pairs)
            kept.append(keep + got.astype(jnp.float32))
        parts = kept
        bit *= 2
    return [p[:, 0, :] for p in parts]


def doubling_gather(rows, n_blk):
    me = lax.axis_index("blk")
    bit = 1
    while bit < n_blk:
        other = lax.ppermute(rows, "blk", [(i, i ^ bit) for i in range(n_blk)])
        low = (me // bit) % 2 == 0
        rows = jnp.where(
            low, jnp.concatenate([rows, other], axis=0), jnp.concatenate([other, rows], axis=0)
        )
        bit *= 2
    return rows


def local(
    audio_frames, conv_weight, proj_weight, text_embed, pair_langs, log_scale, lang_bias, log_var
):
    frames = audio_frames[0]
    text_rows = text_embed[0]
    pair_ids = pair_langs[0]
    local_pairs = frames.shape[0]
    n_blk = lax.axis_size("blk")
    n_dp = lax.axis_size("dp")
    emb = proj_weight.shape[1]
    classes = jnp.arange(log_scale.shape[0], dtype=jnp.int32)
    onehot = (pair_ids[:, None] == classes[None, :]).astype(jnp.float32)
    local_counts = jnp.sum(onehot, axis=0)
    stacked, preact, pooled, audio_unit, audio_len = encode(frames, conv_weight, proj_weight)
    audio_bf = audio_unit.astype(jnp.bfloat16)
    text_unit, text_len = normalize_text(text_rows)
    text_bf = text_unit.astype(jnp.bfloat16)
    id_cols = jnp.broadcast_to(pair_ids.astype(jnp.bfloat16)[:, None], (local_pairs, 128))
    text_packet = jnp.concatenate([text_bf, id_cols], axis=1)
    gathered = lax.all_gather(text_packet, "blk", axis=0, tiled=True)
    counts = local_counts
    for axis, size in (("blk", n_blk), ("dp", n_dp)):
        bit = 1
        while bit < size:
            counts = counts + lax.ppermute(counts, axis, [(i, i ^ bit) for i in range(size)])
            bit *= 2
    all_audio = doubling_gather(audio_bf, n_blk)
    all_text = gathered[:, :emb]
    all_ids = gathered[:, emb].astype(jnp.int32)
    weight_table = jnp.exp(-log_var) / jnp.maximum(counts, 1.0)
    scale_table = jnp.exp(log_scale)
    all_onehot = (all_ids[:, None] == classes[None, :]).astype(jnp.float32)
    pair_scale = jnp.sum(all_onehot * scale_table[None, :], axis=1)
    pair_bias = jnp.sum(all_onehot * lang_bias[None, :], axis=1)
    pair_weight = jnp.sum(all_onehot * weight_table[None, :], axis=1)
    logits = (
        pair_scale[:, None]
        * lax.dot_general(
            all_audio, all_text, (((1,), (1,)), ((), ())), preferred_element_type=jnp.float32
        )
        + pair_bias[:, None]
    )
    row_max = jnp.max(logits, axis=1)
    row_lse = row_max + jnp.log(jnp.sum(jnp.exp(logits - row_max[:, None]), axis=1))
    col_max = jnp.max(logits, axis=0)
    col_lse = col_max + jnp.log(jnp.sum(jnp.exp(logits - col_max[None, :]), axis=0))
    index = jnp.arange(logits.shape[0], dtype=jnp.int32)
    on_diagonal = index[:, None] == index[None, :]
    positive = jnp.sum(jnp.where(on_diagonal, logits, 0.0), axis=1)
    pair_loss = 0.5 * (row_lse + col_lse) - positive
    score_grad = 0.5 * (
        pair_weight[:, None] * jnp.exp(logits - row_lse[:, None])
        + pair_weight[None, :] * jnp.exp(logits - col_lse[None, :])
    )
    score_grad = score_grad - jnp.where(on_diagonal, pair_weight[:, None], 0.0)
    scale_terms = jnp.sum(score_grad * (logits - pair_bias[:, None]), axis=1)
    weighted = (score_grad * pair_scale[:, None]).astype(jnp.bfloat16)
    offset = lax.axis_index("blk") * local_pairs
    own_rows = lax.dynamic_slice_in_dim(weighted, offset, local_pairs, 0)
    own_cols = lax.dynamic_slice_in_dim(weighted, offset, local_pairs, 1)
    grad_audio = jnp.dot(own_rows, all_text, preferred_element_type=jnp.float32)
    grad_text = lax.dot_general(
        own_cols, all_audio, (((0,), (0,)), ((), ())), preferred_element_type=jnp.float32
    )
    text_grad = (
        grad_text - text_unit * jnp.sum(text_unit * grad_text, axis=1, keepdims=True)
    ) / text_len
    batch_sums = jnp.stack(
        [
            jnp.sum(all_onehot * pair_loss[:, None], axis=0),
            jnp.sum(all_onehot * scale_terms[:, None], axis=0),
        ]
    )
    conv_term_t, proj_term_t = encode_back(
        stacked, preact, pooled, audio_unit, audio_len, grad_audio, proj_weight
    )
    buf, per_block = scatter_buffer(conv_term_t, proj_term_t, n_blk, n_dp)
    buf, batch_sums = lax.optimization_barrier((buf, batch_sums))
    stage = lax.psum_scatter(buf, "dp", scatter_dimension=0, tiled=True)
    loss_sum, scale_grad = lax.psum(batch_sums, "dp")
    conv_cols = conv_term_t.shape[0] // n_dp
    conv_part, proj_part = halving_scatter(stage[0], conv_cols, n_blk)
    conv_grad = conv_part.T
    proj_grad = (
        proj_part.reshape(-1)[:per_block]
        .reshape(proj_term_t.shape[0] // n_dp, proj_term_t.shape[1] // n_blk)
        .T
    )
    var_weight = jnp.exp(-log_var)
    lang_mean = loss_sum / jnp.maximum(counts, 1.0)
    loss = jnp.sum(var_weight * lang_mean + log_var)
    var_grad = 1.0 - var_weight * lang_mean
    return (loss, scale_grad, var_grad, conv_grad, proj_grad, text_grad[None])


def solution(mesh):
    return jax.shard_map(
        local,
        mesh=mesh,
        in_specs=(
            P("dp", "blk", None, None),
            P(),
            P(),
            P("dp", "blk", None),
            P("dp", "blk"),
            P(),
            P(),
            P(),
        ),
        out_specs=(P(), P(), P(), P("blk", "dp"), P("blk", "dp"), P("dp", "blk", None)),
        check_vma=False,
    )
```

```python
import jax
import jax.numpy as jnp
from jax import lax
from jax.sharding import PartitionSpec as P

epsilon = 1e-06


def stack_taps(frames):
    clips, steps_count, channels = frames.shape
    blank = jnp.zeros_like(frames[:, :1])
    before = jnp.concatenate([blank, frames[:, :-1]], axis=1)
    after = jnp.concatenate([frames[:, 1:], blank], axis=1)
    return jnp.concatenate([before, frames, after], axis=2).reshape(
        clips * steps_count, 3 * channels
    )


def encode(frames, conv_weight, proj_weight):
    clips, steps_count, channels = frames.shape
    stacked = stack_taps(frames)
    preact = jnp.dot(stacked, conv_weight, preferred_element_type=jnp.float32)
    pooled = jnp.mean(jax.nn.gelu(preact).reshape(clips, steps_count, -1), axis=1).astype(
        jnp.bfloat16
    )
    embedding = jnp.dot(pooled, proj_weight, preferred_element_type=jnp.float32)
    audio_len = jnp.sqrt(jnp.sum(embedding * embedding, axis=-1, keepdims=True) + epsilon)
    return (stacked, preact, pooled, embedding / audio_len, audio_len)


def normalize_text(text_rows):
    text_float = text_rows.astype(jnp.float32)
    text_len = jnp.sqrt(jnp.sum(text_float * text_float, axis=-1, keepdims=True) + epsilon)
    return (text_float / text_len, text_len)


def encode_back(stacked, preact, pooled, audio_unit, audio_len, grad_audio, proj_weight):
    clips = pooled.shape[0]
    steps_count = preact.shape[0] // clips
    radial = jnp.sum(audio_unit * grad_audio, axis=-1, keepdims=True)
    grad_embed = ((grad_audio - audio_unit * radial) / audio_len).astype(jnp.bfloat16)
    proj_term_t = lax.dot_general(
        grad_embed, pooled, (((0,), (0,)), ((), ())), preferred_element_type=jnp.float32
    )
    grad_pooled = (
        lax.dot_general(
            grad_embed, proj_weight, (((1,), (1,)), ((), ())), preferred_element_type=jnp.float32
        )
        / steps_count
    )
    grad_act = jnp.broadcast_to(
        grad_pooled[:, None, :], (clips, steps_count, grad_pooled.shape[1])
    ).reshape(clips * steps_count, -1)
    grad_pre = jax.vjp(jax.nn.gelu, preact)[1](grad_act)[0].astype(jnp.bfloat16)
    conv_term_t = lax.dot_general(
        grad_pre, stacked, (((0,), (0,)), ((), ())), preferred_element_type=jnp.float32
    )
    return (conv_term_t, proj_term_t)


def scatter_buffer(conv_term_t, proj_term_t, n_blk, n_dp):
    width = conv_term_t.shape[1]
    conv_part = conv_term_t.astype(jnp.bfloat16).reshape(n_dp, -1, width)
    p_cols, p_rows = proj_term_t.shape
    per_block = (p_cols // n_dp) * (p_rows // n_blk)
    seg = width // n_blk
    pad_rows = -(-per_block // seg)
    pad_rows = -(-pad_rows // 16) * 16
    proj_part = (
        proj_term_t.astype(jnp.bfloat16)
        .reshape(n_dp, p_cols // n_dp, n_blk, p_rows // n_blk)
        .transpose(0, 2, 1, 3)
        .reshape(n_dp, n_blk, per_block)
    )
    proj_part = jnp.pad(proj_part, ((0, 0), (0, 0), (0, pad_rows * seg - per_block)))
    proj_part = (
        proj_part.reshape(n_dp, n_blk, pad_rows, seg).transpose(0, 2, 1, 3).reshape(n_dp, pad_rows, width)
    )
    return jnp.concatenate([conv_part, proj_part], axis=1), per_block


def halving_scatter(rows, split, n_blk):
    me = lax.axis_index("blk")
    parts = [rows[:split], rows[split:]]
    parts = [p.reshape(p.shape[0], n_blk, -1).astype(jnp.float32) for p in parts]
    bit = 1
    while bit < n_blk:
        mine = (me // bit) % 2
        pairs = [(i, i ^ bit) for i in range(n_blk)]
        kept = []
        for p in parts:
            grouped = p.reshape(p.shape[0], p.shape[1] // 2, 2, p.shape[2])
            keep = lax.dynamic_index_in_dim(grouped, mine, axis=2, keepdims=False)
            send = lax.dynamic_index_in_dim(grouped, 1 - mine, axis=2, keepdims=False)
            got = lax.ppermute(send.astype(jnp.bfloat16), "blk", pairs)
            kept.append(keep + got.astype(jnp.float32))
        parts = kept
        bit *= 2
    return [p[:, 0, :] for p in parts]


def doubling_gather(rows, n_blk):
    me = lax.axis_index("blk")
    bit = 1
    while bit < n_blk:
        other = lax.ppermute(rows, "blk", [(i, i ^ bit) for i in range(n_blk)])
        low = (me // bit) % 2 == 0
        rows = jnp.where(
            low, jnp.concatenate([rows, other], axis=0), jnp.concatenate([other, rows], axis=0)
        )
        bit *= 2
    return rows


def local(
    audio_frames, conv_weight, proj_weight, text_embed, pair_langs, log_scale, lang_bias, log_var
):
    frames = audio_frames[0]
    text_rows = text_embed[0]
    pair_ids = pair_langs[0]
    local_pairs = frames.shape[0]
    n_blk = lax.axis_size("blk")
    n_dp = lax.axis_size("dp")
    emb = proj_weight.shape[1]
    classes = jnp.arange(log_scale.shape[0], dtype=jnp.int32)
    onehot = (pair_ids[:, None] == classes[None, :]).astype(jnp.float32)
    local_counts = jnp.sum(onehot, axis=0)
    stacked, preact, pooled, audio_unit, audio_len = encode(frames, conv_weight, proj_weight)
    audio_bf = audio_unit.astype(jnp.bfloat16)
    text_unit, text_len = normalize_text(text_rows)
    text_bf = text_unit.astype(jnp.bfloat16)
    id_cols = jnp.broadcast_to(pair_ids.astype(jnp.bfloat16)[:, None], (local_pairs, 128))
    text_packet = jnp.concatenate([text_bf, id_cols], axis=1)
    gathered = lax.all_gather(text_packet, "blk", axis=0, tiled=True)
    counts = local_counts
    for axis, size in (("blk", n_blk), ("dp", n_dp)):
        bit = 1
        while bit < size:
            counts = counts + lax.ppermute(counts, axis, [(i, i ^ bit) for i in range(size)])
            bit *= 2
    audio_bf, counts = lax.optimization_barrier((audio_bf, counts))
    all_audio = doubling_gather(audio_bf, n_blk)
    all_text = gathered[:, :emb]
    all_ids = gathered[:, emb].astype(jnp.int32)
    weight_table = jnp.exp(-log_var) / jnp.maximum(counts, 1.0)
    scale_table = jnp.exp(log_scale)
    all_onehot = (all_ids[:, None] == classes[None, :]).astype(jnp.float32)
    pair_scale = jnp.sum(all_onehot * scale_table[None, :], axis=1)
    pair_bias = jnp.sum(all_onehot * lang_bias[None, :], axis=1)
    pair_weight = jnp.sum(all_onehot * weight_table[None, :], axis=1)
    logits = (
        pair_scale[:, None]
        * lax.dot_general(
            all_audio, all_text, (((1,), (1,)), ((), ())), preferred_element_type=jnp.float32
        )
        + pair_bias[:, None]
    )
    row_max = jnp.max(logits, axis=1)
    row_lse = row_max + jnp.log(jnp.sum(jnp.exp(logits - row_max[:, None]), axis=1))
    col_max = jnp.max(logits, axis=0)
    col_lse = col_max + jnp.log(jnp.sum(jnp.exp(logits - col_max[None, :]), axis=0))
    index = jnp.arange(logits.shape[0], dtype=jnp.int32)
    on_diagonal = index[:, None] == index[None, :]
    positive = jnp.sum(jnp.where(on_diagonal, logits, 0.0), axis=1)
    pair_loss = 0.5 * (row_lse + col_lse) - positive
    score_grad = 0.5 * (
        pair_weight[:, None] * jnp.exp(logits - row_lse[:, None])
        + pair_weight[None, :] * jnp.exp(logits - col_lse[None, :])
    )
    score_grad = score_grad - jnp.where(on_diagonal, pair_weight[:, None], 0.0)
    scale_terms = jnp.sum(score_grad * (logits - pair_bias[:, None]), axis=1)
    weighted = (score_grad * pair_scale[:, None]).astype(jnp.bfloat16)
    offset = lax.axis_index("blk") * local_pairs
    own_rows = lax.dynamic_slice_in_dim(weighted, offset, local_pairs, 0)
    own_cols = lax.dynamic_slice_in_dim(weighted, offset, local_pairs, 1)
    grad_audio = jnp.dot(own_rows, all_text, preferred_element_type=jnp.float32)
    grad_text = lax.dot_general(
        own_cols, all_audio, (((0,), (0,)), ((), ())), preferred_element_type=jnp.float32
    )
    text_grad = (
        grad_text - text_unit * jnp.sum(text_unit * grad_text, axis=1, keepdims=True)
    ) / text_len
    batch_sums = jnp.stack(
        [
            jnp.sum(all_onehot * pair_loss[:, None], axis=0),
            jnp.sum(all_onehot * scale_terms[:, None], axis=0),
        ]
    )
    conv_term_t, proj_term_t = encode_back(
        stacked, preact, pooled, audio_unit, audio_len, grad_audio, proj_weight
    )
    buf, per_block = scatter_buffer(conv_term_t, proj_term_t, n_blk, n_dp)
    buf, batch_sums = lax.optimization_barrier((buf, batch_sums))
    stage = lax.psum_scatter(buf, "dp", scatter_dimension=0, tiled=True)
    loss_sum, scale_grad = lax.psum(batch_sums, "dp")
    conv_cols = conv_term_t.shape[0] // n_dp
    conv_part, proj_part = halving_scatter(stage[0], conv_cols, n_blk)
    conv_grad = conv_part.T
    proj_grad = (
        proj_part.reshape(-1)[:per_block]
        .reshape(proj_term_t.shape[0] // n_dp, proj_term_t.shape[1] // n_blk)
        .T
    )
    var_weight = jnp.exp(-log_var)
    lang_mean = loss_sum / jnp.maximum(counts, 1.0)
    loss = jnp.sum(var_weight * lang_mean + log_var)
    var_grad = 1.0 - var_weight * lang_mean
    return (loss, scale_grad, var_grad, conv_grad, proj_grad, text_grad[None])


def solution(mesh):
    return jax.shard_map(
        local,
        mesh=mesh,
        in_specs=(
            P("dp", "blk", None, None),
            P(),
            P(),
            P("dp", "blk", None),
            P("dp", "blk"),
            P(),
            P(),
            P(),
        ),
        out_specs=(P(), P(), P(), P("blk", "dp"), P("blk", "dp"), P("dp", "blk", None)),
        check_vma=False,
    )
```

```python
import jax
import jax.numpy as jnp
from jax import lax
from jax.sharding import PartitionSpec as P

epsilon = 1e-06


def stack_taps(frames):
    clips, steps_count, channels = frames.shape
    blank = jnp.zeros_like(frames[:, :1])
    before = jnp.concatenate([blank, frames[:, :-1]], axis=1)
    after = jnp.concatenate([frames[:, 1:], blank], axis=1)
    return jnp.concatenate([before, frames, after], axis=2).reshape(
        clips * steps_count, 3 * channels
    )


def encode(frames, conv_weight, proj_weight):
    clips, steps_count, channels = frames.shape
    stacked = stack_taps(frames)
    preact = jnp.dot(stacked, conv_weight, preferred_element_type=jnp.float32)
    pooled = jnp.mean(jax.nn.gelu(preact).reshape(clips, steps_count, -1), axis=1).astype(
        jnp.bfloat16
    )
    embedding = jnp.dot(pooled, proj_weight, preferred_element_type=jnp.float32)
    audio_len = jnp.sqrt(jnp.sum(embedding * embedding, axis=-1, keepdims=True) + epsilon)
    return (stacked, preact, pooled, embedding / audio_len, audio_len)


def normalize_text(text_rows):
    text_float = text_rows.astype(jnp.float32)
    text_len = jnp.sqrt(jnp.sum(text_float * text_float, axis=-1, keepdims=True) + epsilon)
    return (text_float / text_len, text_len)


def encode_back(stacked, preact, pooled, audio_unit, audio_len, grad_audio, proj_weight, n_blk):
    clips = pooled.shape[0]
    steps_count = preact.shape[0] // clips
    radial = jnp.sum(audio_unit * grad_audio, axis=-1, keepdims=True)
    grad_embed = ((grad_audio - audio_unit * radial) / audio_len).astype(jnp.bfloat16)
    width = pooled.shape[1]
    pooled_perm = pooled.reshape(clips, n_blk, 2, width // n_blk // 2).transpose(0, 2, 1, 3)
    proj_term_t = lax.dot_general(
        grad_embed,
        pooled_perm.reshape(clips, width),
        (((0,), (0,)), ((), ())),
        preferred_element_type=jnp.float32,
    )
    grad_pooled = (
        lax.dot_general(
            grad_embed, proj_weight, (((1,), (1,)), ((), ())), preferred_element_type=jnp.float32
        )
        / steps_count
    )
    grad_act = jnp.broadcast_to(
        grad_pooled[:, None, :], (clips, steps_count, grad_pooled.shape[1])
    ).reshape(clips * steps_count, -1)
    grad_pre = jax.vjp(jax.nn.gelu, preact)[1](grad_act)[0].astype(jnp.bfloat16)
    conv_term_t = lax.dot_general(
        grad_pre, stacked, (((0,), (0,)), ((), ())), preferred_element_type=jnp.float32
    )
    return (conv_term_t, proj_term_t)


def scatter_buffer(conv_term_t, proj_term_t, n_dp):
    conv_part = conv_term_t.astype(jnp.bfloat16).reshape(n_dp, -1, conv_term_t.shape[1])
    rows = conv_part.shape[1]
    proj_part = proj_term_t.astype(jnp.bfloat16).reshape(n_dp, rows, -1)
    return jnp.concatenate([conv_part, proj_part], axis=2)


def halving_scatter(parts, n_blk):
    me = lax.axis_index("blk")
    parts = [p.reshape(p.shape[0], n_blk, -1).astype(jnp.float32) for p in parts]
    bit = 1
    while bit < n_blk:
        mine = (me // bit) % 2
        pairs = [(i, i ^ bit) for i in range(n_blk)]
        kept = []
        for p in parts:
            grouped = p.reshape(p.shape[0], p.shape[1] // 2, 2, p.shape[2])
            keep = lax.dynamic_index_in_dim(grouped, mine, axis=2, keepdims=False)
            send = lax.dynamic_index_in_dim(grouped, 1 - mine, axis=2, keepdims=False)
            got = lax.ppermute(send.astype(jnp.bfloat16), "blk", pairs)
            kept.append(keep + got.astype(jnp.float32))
        parts = kept
        bit *= 2
    return [p[:, 0, :] for p in parts]


def local(
    audio_frames, conv_weight, proj_weight, text_embed, pair_langs, log_scale, lang_bias, log_var
):
    frames = audio_frames[0]
    text_rows = text_embed[0]
    pair_ids = pair_langs[0]
    local_pairs = frames.shape[0]
    n_blk = lax.axis_size("blk")
    n_dp = lax.axis_size("dp")
    emb = proj_weight.shape[1]
    classes = jnp.arange(log_scale.shape[0], dtype=jnp.int32)
    onehot = (pair_ids[:, None] == classes[None, :]).astype(jnp.float32)
    local_counts = jnp.sum(onehot, axis=0)
    stacked, preact, pooled, audio_unit, audio_len = encode(frames, conv_weight, proj_weight)
    audio_bf = audio_unit.astype(jnp.bfloat16)
    text_unit, text_len = normalize_text(text_rows)
    text_bf = text_unit.astype(jnp.bfloat16)
    id_cols = jnp.broadcast_to(pair_ids.astype(jnp.bfloat16)[:, None], (local_pairs, 128))
    packet = jnp.concatenate([audio_bf, text_bf, id_cols], axis=1)
    packet, local_counts = lax.optimization_barrier((packet, local_counts))
    gathered = lax.all_gather(packet, "blk", axis=0, tiled=True)
    counts = lax.psum(local_counts, ("blk", "dp"))
    all_audio = gathered[:, :emb]
    all_text = gathered[:, emb : 2 * emb]
    all_ids = gathered[:, 2 * emb].astype(jnp.int32)
    weight_table = jnp.exp(-log_var) / jnp.maximum(counts, 1.0)
    scale_table = jnp.exp(log_scale)
    all_onehot = (all_ids[:, None] == classes[None, :]).astype(jnp.float32)
    pair_scale = jnp.sum(all_onehot * scale_table[None, :], axis=1)
    pair_bias = jnp.sum(all_onehot * lang_bias[None, :], axis=1)
    pair_weight = jnp.sum(all_onehot * weight_table[None, :], axis=1)
    logits = (
        pair_scale[:, None]
        * lax.dot_general(
            all_audio, all_text, (((1,), (1,)), ((), ())), preferred_element_type=jnp.float32
        )
        + pair_bias[:, None]
    )
    row_max = jnp.max(logits, axis=1)
    row_lse = row_max + jnp.log(jnp.sum(jnp.exp(logits - row_max[:, None]), axis=1))
    col_max = jnp.max(logits, axis=0)
    col_lse = col_max + jnp.log(jnp.sum(jnp.exp(logits - col_max[None, :]), axis=0))
    index = jnp.arange(logits.shape[0], dtype=jnp.int32)
    on_diagonal = index[:, None] == index[None, :]
    positive = jnp.sum(jnp.where(on_diagonal, logits, 0.0), axis=1)
    pair_loss = 0.5 * (row_lse + col_lse) - positive
    score_grad = 0.5 * (
        pair_weight[:, None] * jnp.exp(logits - row_lse[:, None])
        + pair_weight[None, :] * jnp.exp(logits - col_lse[None, :])
    )
    score_grad = score_grad - jnp.where(on_diagonal, pair_weight[:, None], 0.0)
    scale_terms = jnp.sum(score_grad * (logits - pair_bias[:, None]), axis=1)
    weighted = (score_grad * pair_scale[:, None]).astype(jnp.bfloat16)
    offset = lax.axis_index("blk") * local_pairs
    own_rows = lax.dynamic_slice_in_dim(weighted, offset, local_pairs, 0)
    own_cols = lax.dynamic_slice_in_dim(weighted, offset, local_pairs, 1)
    grad_audio = jnp.dot(own_rows, all_text, preferred_element_type=jnp.float32)
    grad_text = lax.dot_general(
        own_cols, all_audio, (((0,), (0,)), ((), ())), preferred_element_type=jnp.float32
    )
    text_grad = (
        grad_text - text_unit * jnp.sum(text_unit * grad_text, axis=1, keepdims=True)
    ) / text_len
    batch_sums = jnp.stack(
        [
            jnp.sum(all_onehot * pair_loss[:, None], axis=0),
            jnp.sum(all_onehot * scale_terms[:, None], axis=0),
        ]
    )
    conv_term_t, proj_term_t = encode_back(
        stacked, preact, pooled, audio_unit, audio_len, grad_audio, proj_weight, n_blk
    )
    buf = scatter_buffer(conv_term_t, proj_term_t, n_dp)
    buf, batch_sums = lax.optimization_barrier((buf, batch_sums))
    stage = lax.psum_scatter(buf, "dp", scatter_dimension=0, tiled=True)
    loss_sum, scale_grad = lax.psum(batch_sums, "dp")
    conv_width = conv_term_t.shape[1]
    conv_part, proj_part = halving_scatter(
        [stage[0, :, :conv_width], stage[0, :, conv_width:]], n_blk
    )
    conv_grad = conv_part.T
    proj_cols = proj_term_t.shape[0] // n_dp
    proj_grad = (
        proj_part.reshape(proj_cols, 2, -1).transpose(1, 2, 0).reshape(-1, proj_cols)
    )
    var_weight = jnp.exp(-log_var)
    lang_mean = loss_sum / jnp.maximum(counts, 1.0)
    loss = jnp.sum(var_weight * lang_mean + log_var)
    var_grad = 1.0 - var_weight * lang_mean
    return (loss, scale_grad, var_grad, conv_grad, proj_grad, text_grad[None])


def solution(mesh):
    return jax.shard_map(
        local,
        mesh=mesh,
        in_specs=(
            P("dp", "blk", None, None),
            P(),
            P(),
            P("dp", "blk", None),
            P("dp", "blk"),
            P(),
            P(),
            P(),
        ),
        out_specs=(P(), P(), P(), P("blk", "dp"), P("blk", "dp"), P("dp", "blk", None)),
        check_vma=False,
    )
```

```python
import jax
import jax.numpy as jnp
from jax import lax
from jax.sharding import PartitionSpec as P

epsilon = 1e-06


def stack_taps(frames):
    clips, steps_count, channels = frames.shape
    blank = jnp.zeros_like(frames[:, :1])
    before = jnp.concatenate([blank, frames[:, :-1]], axis=1)
    after = jnp.concatenate([frames[:, 1:], blank], axis=1)
    return jnp.concatenate([before, frames, after], axis=2).reshape(
        clips * steps_count, 3 * channels
    )


def encode(frames, conv_weight, proj_weight):
    clips, steps_count, channels = frames.shape
    stacked = stack_taps(frames)
    preact = jnp.dot(stacked, conv_weight, preferred_element_type=jnp.float32)
    pooled = jnp.mean(jax.nn.gelu(preact).reshape(clips, steps_count, -1), axis=1).astype(
        jnp.bfloat16
    )
    embedding = jnp.dot(pooled, proj_weight, preferred_element_type=jnp.float32)
    audio_len = jnp.sqrt(jnp.sum(embedding * embedding, axis=-1, keepdims=True) + epsilon)
    return (stacked, preact, pooled, embedding / audio_len, audio_len)


def normalize_text(text_rows):
    text_float = text_rows.astype(jnp.float32)
    text_len = jnp.sqrt(jnp.sum(text_float * text_float, axis=-1, keepdims=True) + epsilon)
    return (text_float / text_len, text_len)


def encode_back(stacked, preact, pooled, audio_unit, audio_len, grad_audio, proj_weight, n_blk):
    clips = pooled.shape[0]
    steps_count = preact.shape[0] // clips
    radial = jnp.sum(audio_unit * grad_audio, axis=-1, keepdims=True)
    grad_embed = ((grad_audio - audio_unit * radial) / audio_len).astype(jnp.bfloat16)
    width = pooled.shape[1]
    pooled_perm = pooled.reshape(clips, n_blk, 2, width // n_blk // 2).transpose(0, 2, 1, 3)
    proj_term_t = lax.dot_general(
        grad_embed,
        pooled_perm.reshape(clips, width),
        (((0,), (0,)), ((), ())),
        preferred_element_type=jnp.float32,
    )
    grad_pooled = (
        lax.dot_general(
            grad_embed, proj_weight, (((1,), (1,)), ((), ())), preferred_element_type=jnp.float32
        )
        / steps_count
    )
    grad_act = jnp.broadcast_to(
        grad_pooled[:, None, :], (clips, steps_count, grad_pooled.shape[1])
    ).reshape(clips * steps_count, -1)
    grad_pre = jax.vjp(jax.nn.gelu, preact)[1](grad_act)[0].astype(jnp.bfloat16)
    conv_term_t = lax.dot_general(
        grad_pre, stacked, (((0,), (0,)), ((), ())), preferred_element_type=jnp.float32
    )
    return (conv_term_t, proj_term_t)


def scatter_buffer(conv_term_t, proj_term_t, n_dp):
    conv_part = conv_term_t.astype(jnp.bfloat16).reshape(n_dp, -1, conv_term_t.shape[1])
    rows = conv_part.shape[1]
    proj_part = proj_term_t.astype(jnp.bfloat16).reshape(n_dp, rows, -1)
    return jnp.concatenate([conv_part, proj_part], axis=2)


def halving_scatter(parts, n_blk):
    me = lax.axis_index("blk")
    segs = [p.shape[1] // n_blk for p in parts]
    parts = [
        jnp.concatenate(
            [p.reshape(p.shape[0], n_blk, -1) for p in parts], axis=2
        ).astype(jnp.float32)
    ]
    bit = 1
    while bit < n_blk:
        mine = (me // bit) % 2
        pairs = [(i, i ^ bit) for i in range(n_blk)]
        kept = []
        for p in parts:
            grouped = p.reshape(p.shape[0], p.shape[1] // 2, 2, p.shape[2])
            keep = lax.dynamic_index_in_dim(grouped, mine, axis=2, keepdims=False)
            send = lax.dynamic_index_in_dim(grouped, 1 - mine, axis=2, keepdims=False)
            got = lax.ppermute(send.astype(jnp.bfloat16), "blk", pairs)
            kept.append(keep + got.astype(jnp.float32))
        parts = kept
        bit *= 2
    joined = parts[0][:, 0, :]
    return [joined[:, : segs[0]], joined[:, segs[0] :]]


def local(
    audio_frames, conv_weight, proj_weight, text_embed, pair_langs, log_scale, lang_bias, log_var
):
    frames = audio_frames[0]
    text_rows = text_embed[0]
    pair_ids = pair_langs[0]
    local_pairs = frames.shape[0]
    n_blk = lax.axis_size("blk")
    n_dp = lax.axis_size("dp")
    emb = proj_weight.shape[1]
    classes = jnp.arange(log_scale.shape[0], dtype=jnp.int32)
    onehot = (pair_ids[:, None] == classes[None, :]).astype(jnp.float32)
    local_counts = jnp.sum(onehot, axis=0)
    stacked, preact, pooled, audio_unit, audio_len = encode(frames, conv_weight, proj_weight)
    audio_bf = audio_unit.astype(jnp.bfloat16)
    text_unit, text_len = normalize_text(text_rows)
    text_bf = text_unit.astype(jnp.bfloat16)
    id_cols = jnp.broadcast_to(pair_ids.astype(jnp.bfloat16)[:, None], (local_pairs, 128))
    packet = jnp.concatenate([audio_bf, text_bf, id_cols], axis=1)
    packet, local_counts = lax.optimization_barrier((packet, local_counts))
    gathered = lax.all_gather(packet, "blk", axis=0, tiled=True)
    counts = lax.psum(local_counts, ("blk", "dp"))
    all_audio = gathered[:, :emb]
    all_text = gathered[:, emb : 2 * emb]
    all_ids = gathered[:, 2 * emb].astype(jnp.int32)
    weight_table = jnp.exp(-log_var) / jnp.maximum(counts, 1.0)
    scale_table = jnp.exp(log_scale)
    all_onehot = (all_ids[:, None] == classes[None, :]).astype(jnp.float32)
    pair_scale = jnp.sum(all_onehot * scale_table[None, :], axis=1)
    pair_bias = jnp.sum(all_onehot * lang_bias[None, :], axis=1)
    pair_weight = jnp.sum(all_onehot * weight_table[None, :], axis=1)
    logits = (
        pair_scale[:, None]
        * lax.dot_general(
            all_audio, all_text, (((1,), (1,)), ((), ())), preferred_element_type=jnp.float32
        )
        + pair_bias[:, None]
    )
    row_max = jnp.max(logits, axis=1)
    row_lse = row_max + jnp.log(jnp.sum(jnp.exp(logits - row_max[:, None]), axis=1))
    col_max = jnp.max(logits, axis=0)
    col_lse = col_max + jnp.log(jnp.sum(jnp.exp(logits - col_max[None, :]), axis=0))
    index = jnp.arange(logits.shape[0], dtype=jnp.int32)
    on_diagonal = index[:, None] == index[None, :]
    positive = jnp.sum(jnp.where(on_diagonal, logits, 0.0), axis=1)
    pair_loss = 0.5 * (row_lse + col_lse) - positive
    score_grad = 0.5 * (
        pair_weight[:, None] * jnp.exp(logits - row_lse[:, None])
        + pair_weight[None, :] * jnp.exp(logits - col_lse[None, :])
    )
    score_grad = score_grad - jnp.where(on_diagonal, pair_weight[:, None], 0.0)
    scale_terms = jnp.sum(score_grad * (logits - pair_bias[:, None]), axis=1)
    weighted = (score_grad * pair_scale[:, None]).astype(jnp.bfloat16)
    offset = lax.axis_index("blk") * local_pairs
    own_rows = lax.dynamic_slice_in_dim(weighted, offset, local_pairs, 0)
    own_cols = lax.dynamic_slice_in_dim(weighted, offset, local_pairs, 1)
    grad_audio = jnp.dot(own_rows, all_text, preferred_element_type=jnp.float32)
    grad_text = lax.dot_general(
        own_cols, all_audio, (((0,), (0,)), ((), ())), preferred_element_type=jnp.float32
    )
    text_grad = (
        grad_text - text_unit * jnp.sum(text_unit * grad_text, axis=1, keepdims=True)
    ) / text_len
    batch_sums = jnp.stack(
        [
            jnp.sum(all_onehot * pair_loss[:, None], axis=0),
            jnp.sum(all_onehot * scale_terms[:, None], axis=0),
        ]
    )
    conv_term_t, proj_term_t = encode_back(
        stacked, preact, pooled, audio_unit, audio_len, grad_audio, proj_weight, n_blk
    )
    buf = scatter_buffer(conv_term_t, proj_term_t, n_dp)
    buf, batch_sums = lax.optimization_barrier((buf, batch_sums))
    stage = lax.psum_scatter(buf, "dp", scatter_dimension=0, tiled=True)
    loss_sum, scale_grad = lax.psum(batch_sums, "dp")
    conv_width = conv_term_t.shape[1]
    conv_part, proj_part = halving_scatter(
        [stage[0, :, :conv_width], stage[0, :, conv_width:]], n_blk
    )
    conv_grad = conv_part.T
    proj_cols = proj_term_t.shape[0] // n_dp
    proj_grad = (
        proj_part.reshape(proj_cols, 2, -1).transpose(1, 2, 0).reshape(-1, proj_cols)
    )
    var_weight = jnp.exp(-log_var)
    lang_mean = loss_sum / jnp.maximum(counts, 1.0)
    loss = jnp.sum(var_weight * lang_mean + log_var)
    var_grad = 1.0 - var_weight * lang_mean
    return (loss, scale_grad, var_grad, conv_grad, proj_grad, text_grad[None])


def solution(mesh):
    return jax.shard_map(
        local,
        mesh=mesh,
        in_specs=(
            P("dp", "blk", None, None),
            P(),
            P(),
            P("dp", "blk", None),
            P("dp", "blk"),
            P(),
            P(),
            P(),
        ),
        out_specs=(P(), P(), P(), P("blk", "dp"), P("blk", "dp"), P("dp", "blk", None)),
        check_vma=False,
    )
```
